128 devices in a mesh: row: 8 (over z_hi, x), col: 16 (over z_lo, y, core).
Axes of the slice: x: 4, y: 4, z: 4 (z_hi: 2, z_lo: 2; z = z_hi * 2 + z_lo), core: 2. Of those that a mesh axis runs over, the one named last changes fastest.
Arguments:
- tokens: bfloat16 [1024, 8192], P(('row', 'col')), may hold values from -6 to 6
- gain: float32 [8192], replicated, may hold values from 0.5 to 1.5
- grad_out: bfloat16 [1024, 8192], P(('row', 'col')), may hold values from -4 to 4
- pre_gate: bfloat16 [1024, 28672], P('col', 'row'), may hold values from -6 to 6
- pre_up: bfloat16 [1024, 28672], P('col', 'row'), may hold values from -6 to 6
- gate_weight: bfloat16 [8192, 28672], P('col', 'row'), may hold values from -0.0625 to 0.0625
- up_weight: bfloat16 [8192, 28672], P('col', 'row'), may hold values from -0.0625 to 0.0625
- down_weight: bfloat16 [28672, 8192], P('row', 'col'), may hold values from -0.03125 to 0.03125
Outputs:
- grad_tokens: bfloat16 [1024, 8192], P(('row', 'col'))
- grad_gain: float32 [8192], replicated
- grad_gate: bfloat16 [8192, 28672], P('col', 'row')
- grad_up: bfloat16 [8192, 28672], P('col', 'row')
- grad_down: bfloat16 [28672, 8192], P('row', 'col')
The draws below stay inside these ranges and needn't reach their ends.
All inputs are finite; a program needn't handle non-finite values.
Results may differ from the reference program's by a relative error of at most 0.0057.
Values may be sent and summed in bfloat16 or wider, within the bound.
No kernel may reach another device: no remote copies, remote signals or barrier semaphores. Data moves between devices by JAX's collectives and lax.ppermute only.
A program may use at most 192 MiB of HBM per device.

```python
import jax
import jax.numpy as jnp
from jax import lax

D = 8192
FF = 28672
TOKENS = 1024


def block_levels(key, extent, cuts, least, top_value):
    level, own = 1.0, jax.random.fold_in(key, 6)
    for dim, parts in cuts:
        steps = jnp.exp(jax.random.uniform(jax.random.fold_in(own, dim), (parts,), jnp.float32, least / len(cuts), top_value / len(cuts)))
        level = level * jnp.repeat(steps, extent[dim] // parts).reshape([-1 if axis == dim else 1 for axis in range(len(extent))])
    return level


def normal_values(rng, extent, scale, limit, pieces=(), held_as=jnp.bfloat16):
    level = block_levels(rng, extent, pieces, -0.22, 0.18) if pieces else 1.0
    entries = jax.random.normal(rng, extent, jnp.float32) * scale * level
    return jnp.minimum(jnp.maximum(entries, -limit), limit).astype(held_as)


def setup_inputs(seed: int = 0) -> dict:
    splits = jax.random.split(jax.random.key(seed), 9)
    tokens = normal_values(splits[0], (TOKENS, D), 1.0, 6.0, ((0, 128),))
    gain = jnp.clip(1.0 + 0.1 * jax.random.normal(splits[1], (D,), jnp.float32), 0.5, 1.5)
    grad_out = normal_values(splits[2], (TOKENS, D), 0.25, 4.0, ((0, 128),))
    pre_gate = normal_values(splits[3], (TOKENS, FF), 1.5, 6.0, ((0, 16), (1, 8)))
    pre_up = normal_values(splits[4], (TOKENS, FF), 1.0, 6.0, ((0, 16), (1, 8)))
    gate_weight = normal_values(splits[5], (D, FF), D ** -0.5, 0.0625, ((0, 16), (1, 8)))
    up_weight = normal_values(splits[6], (D, FF), D ** -0.5, 0.0625, ((0, 16), (1, 8)))
    down_weight = normal_values(splits[7], (FF, D), FF ** -0.5, 0.03125, ((0, 8), (1, 16)))
    return dict(tokens=tokens, gain=gain, grad_out=grad_out, pre_gate=pre_gate, pre_up=pre_up, gate_weight=gate_weight, up_weight=up_weight, down_weight=down_weight)


epsilon = 1e-05

def swiglu_grads(hidden_grad, pre_gate, pre_up):
    gate_wide = pre_gate.astype(jnp.float32)
    up_wide = pre_up.astype(jnp.float32)
    sigmoid = jax.nn.sigmoid(gate_wide)
    silu = gate_wide * sigmoid
    hidden = (silu * up_wide).astype(jnp.bfloat16)
    up_grad = (hidden_grad * silu).astype(jnp.bfloat16)
    gate_grad = (hidden_grad * up_wide * sigmoid * (1.0 + gate_wide * (1.0 - sigmoid))).astype(jnp.bfloat16)
    return (hidden, gate_grad, up_grad)

def reference(tokens, gain, grad_out, pre_gate, pre_up, gate_weight, up_weight, down_weight):
    tokens_wide = tokens.astype(jnp.float32)
    inverse_rms = lax.rsqrt(lax.optimization_barrier(jnp.mean(tokens_wide * tokens_wide, axis=1, keepdims=True)) + epsilon)
    normed = tokens_wide * inverse_rms
    scaled = (normed * gain).astype(jnp.bfloat16)
    hidden_grad = jnp.dot(grad_out, down_weight.T, preferred_element_type=jnp.float32)
    hidden, gate_grad, up_grad = swiglu_grads(hidden_grad, pre_gate, pre_up)
    grad_down = jnp.dot(hidden.T, grad_out, preferred_element_type=jnp.float32).astype(jnp.bfloat16)
    grad_gate = jnp.dot(scaled.T, gate_grad, preferred_element_type=jnp.float32).astype(jnp.bfloat16)
    grad_up = jnp.dot(scaled.T, up_grad, preferred_element_type=jnp.float32).astype(jnp.bfloat16)
    normed_grad = jnp.dot(gate_grad, gate_weight.T, preferred_element_type=jnp.float32) + jnp.dot(up_grad, up_weight.T, preferred_element_type=jnp.float32)
    grad_gain = lax.optimization_barrier(jnp.sum(normed_grad * normed, axis=0))
    scaled_grad = normed_grad * gain
    inner = lax.optimization_barrier(jnp.mean(scaled_grad * normed, axis=1, keepdims=True))
    grad_tokens = (grad_out.astype(jnp.float32) + inverse_rms * (scaled_grad - normed * inner)).astype(jnp.bfloat16)
    return (grad_tokens, grad_gain, grad_gate, grad_up, grad_down)
```

```python
import jax
import jax.numpy as jnp
from jax import lax
from jax.sharding import PartitionSpec as P

epsilon = 1e-05


def swiglu_grads(hidden_grad, pre_gate, pre_up):
    gate_wide = pre_gate.astype(jnp.float32)
    up_wide = pre_up.astype(jnp.float32)
    sigmoid = jax.nn.sigmoid(gate_wide)
    silu = gate_wide * sigmoid
    hidden = (silu * up_wide).astype(jnp.bfloat16)
    up_grad = (hidden_grad * silu).astype(jnp.bfloat16)
    gate_grad = (hidden_grad * up_wide * sigmoid * (1.0 + gate_wide * (1.0 - sigmoid))).astype(
        jnp.bfloat16
    )
    return (hidden, gate_grad, up_grad)


def local(tokens, gain, grad_out, pre_gate, pre_up, gate_weight, up_weight, down_weight):
    tokens_wide = tokens.astype(jnp.float32)
    inverse_rms = lax.rsqrt(jnp.mean(tokens_wide * tokens_wide, axis=1, keepdims=True) + epsilon)
    normed = tokens_wide * inverse_rms
    scaled = (normed * gain).astype(jnp.bfloat16)
    grid_input, grid_grad = (
        lax.all_to_all(scaled, "col", split_axis=1, concat_axis=0, tiled=True),
        lax.all_to_all(grad_out, "col", split_axis=1, concat_axis=0, tiled=True),
    )
    all_input, all_grad = (
        lax.all_gather(grid_input, "row", axis=0, tiled=True),
        lax.all_gather(grid_grad, "row", axis=0, tiled=True),
    )
    partial_grad = jnp.einsum(
        "td,fd->tf", all_grad, down_weight, preferred_element_type=jnp.float32
    )
    block_grad = lax.psum_scatter(partial_grad, "col", scatter_dimension=0, tiled=True)
    hidden_block, gate_block, up_block = swiglu_grads(block_grad, pre_gate, pre_up)
    gate_piece = lax.all_gather(gate_block, "col", axis=0, tiled=True)
    up_piece = lax.all_gather(up_block, "col", axis=0, tiled=True)
    hidden_piece = lax.all_gather(hidden_block, "col", axis=0, tiled=True)
    new_rows = jnp.einsum("tf,df->td", gate_piece, gate_weight, preferred_element_type=jnp.float32)
    new_rows = new_rows + jnp.einsum(
        "tf,df->td", up_piece, up_weight, preferred_element_type=jnp.float32
    )
    gate_total = jnp.einsum("td,tf->df", all_input, gate_piece, preferred_element_type=jnp.float32)
    up_total = jnp.einsum("td,tf->df", all_input, up_piece, preferred_element_type=jnp.float32)
    down_total = jnp.einsum("tf,td->fd", hidden_piece, all_grad, preferred_element_type=jnp.float32)
    grid_back = lax.psum_scatter(new_rows, "row", scatter_dimension=0, tiled=True)
    normed_grad = lax.all_to_all(grid_back, "col", split_axis=0, concat_axis=1, tiled=True)
    gain_terms = jnp.sum(normed_grad * normed, axis=0)
    grad_gain = lax.psum(lax.psum(gain_terms, "col"), "row")
    scaled_grad = normed_grad * gain
    inner = jnp.mean(scaled_grad * normed, axis=1, keepdims=True)
    grad_tokens = (
        grad_out.astype(jnp.float32) + inverse_rms * (scaled_grad - normed * inner)
    ).astype(jnp.bfloat16)
    return (
        grad_tokens,
        grad_gain,
        gate_total.astype(jnp.bfloat16),
        up_total.astype(jnp.bfloat16),
        down_total.astype(jnp.bfloat16),
    )


def solution(mesh):
    in_specs = (
        P(("row", "col"), None),
        P(),
        P(("row", "col"), None),
        P("col", "row"),
        P("col", "row"),
        P("col", "row"),
        P("col", "row"),
        P("row", "col"),
    )
    out_specs = (P(("row", "col"), None), P(), P("col", "row"), P("col", "row"), P("row", "col"))
    return jax.shard_map(local, mesh=mesh, in_specs=in_specs, out_specs=out_specs, check_vma=False)
```

```python
import jax
import jax.numpy as jnp
from jax import lax
from jax.sharding import PartitionSpec as P

epsilon = 1e-05


def swiglu_grads(hidden_grad, pre_gate, pre_up):
    gate_wide = pre_gate.astype(jnp.float32)
    up_wide = pre_up.astype(jnp.float32)
    sigmoid = jax.nn.sigmoid(gate_wide)
    silu = gate_wide * sigmoid
    hidden = (silu * up_wide).astype(jnp.bfloat16)
    up_grad = (hidden_grad * silu).astype(jnp.bfloat16)
    gate_grad = (hidden_grad * up_wide * sigmoid * (1.0 + gate_wide * (1.0 - sigmoid))).astype(
        jnp.bfloat16
    )
    return (hidden, gate_grad, up_grad)


def row_gather(x):
    rows = lax.axis_size("row")
    copies = jnp.broadcast_to(x[None], (rows,) + x.shape)
    got = lax.all_to_all(copies, "row", split_axis=0, concat_axis=0, tiled=True)
    return got.reshape((rows * x.shape[0],) + x.shape[1:])


def local(tokens, gain, grad_out, pre_gate, pre_up, gate_weight, up_weight, down_weight):
    cols = lax.axis_size("col")
    rows = lax.axis_size("row")
    tokens_wide = tokens.astype(jnp.float32)
    inverse_rms = lax.rsqrt(jnp.mean(tokens_wide * tokens_wide, axis=1, keepdims=True) + epsilon)
    normed = tokens_wide * inverse_rms
    tile = gate_weight.shape[0]
    gain_tile = lax.dynamic_slice_in_dim(gain, lax.axis_index("col") * tile, tile)
    grid_normed = lax.all_to_all(normed, "col", split_axis=1, concat_axis=0, tiled=True)
    grid_grad = lax.all_to_all(grad_out, "col", split_axis=1, concat_axis=0, tiled=True)
    all_grad = row_gather(grid_grad)
    partial_grad = jnp.einsum(
        "td,fd->tf", all_grad, down_weight, preferred_element_type=jnp.float32
    )
    block_grad = lax.psum_scatter(partial_grad, "col", scatter_dimension=0, tiled=True)
    hidden_block, gate_block, up_block = swiglu_grads(block_grad, pre_gate, pre_up)
    gate_piece = lax.all_gather(gate_block, "col", axis=0, tiled=True)
    up_piece = lax.all_gather(up_block, "col", axis=0, tiled=True)
    hidden_piece = lax.all_gather(hidden_block, "col", axis=0, tiled=True)
    all_normed = row_gather(grid_normed)
    all_input = (all_normed * gain_tile).astype(jnp.bfloat16)
    new_rows = jnp.einsum("tf,df->td", gate_piece, gate_weight, preferred_element_type=jnp.float32)
    new_rows = new_rows + jnp.einsum(
        "tf,df->td", up_piece, up_weight, preferred_element_type=jnp.float32
    )
    gain_part = jnp.sum(new_rows * all_normed, axis=0)
    tokens_all = new_rows.shape[0]
    blocks = new_rows.reshape(rows, tokens_all // rows, tile)
    extra = jnp.zeros((rows, 8, tile), jnp.float32).at[:, 0, :].set(gain_part)
    sent = jnp.concatenate([blocks, extra], axis=1)
    got = lax.all_to_all(sent, "row", split_axis=0, concat_axis=0, tiled=True)
    summed = jnp.sum(got, axis=0)
    grid_back = summed[: tokens_all // rows]
    gain_tile_grad = summed[tokens_all // rows]
    per_col = grid_back.reshape(cols, -1, tile)
    mine = per_col.shape[1]
    sent2 = jnp.concatenate(
        [per_col, jnp.broadcast_to(gain_tile_grad[None, None, :], (cols, 1, tile))], axis=1
    )
    got2 = lax.all_to_all(sent2, "col", split_axis=0, concat_axis=0, tiled=True)
    normed_grad = got2[:, :mine, :].transpose(1, 0, 2).reshape(mine, cols * tile)
    grad_gain = got2[:, mine, :].reshape(cols * tile)
    gate_total = jnp.einsum("td,tf->df", all_input, gate_piece, preferred_element_type=jnp.float32)
    up_total = jnp.einsum("td,tf->df", all_input, up_piece, preferred_element_type=jnp.float32)
    down_total = jnp.einsum("tf,td->fd", hidden_piece, all_grad, preferred_element_type=jnp.float32)
    scaled_grad = normed_grad * gain
    inner = jnp.mean(scaled_grad * normed, axis=1, keepdims=True)
    grad_tokens = (
        grad_out.astype(jnp.float32) + inverse_rms * (scaled_grad - normed * inner)
    ).astype(jnp.bfloat16)
    return (
        grad_tokens,
        grad_gain,
        gate_total.astype(jnp.bfloat16),
        up_total.astype(jnp.bfloat16),
        down_total.astype(jnp.bfloat16),
    )


def solution(mesh):
    in_specs = (
        P(("row", "col"), None),
        P(),
        P(("row", "col"), None),
        P("col", "row"),
        P("col", "row"),
        P("col", "row"),
        P("col", "row"),
        P("row", "col"),
    )
    out_specs = (P(("row", "col"), None), P(), P("col", "row"), P("col", "row"), P("row", "col"))
    return jax.shard_map(local, mesh=mesh, in_specs=in_specs, out_specs=out_specs, check_vma=False)
```

```python
import jax
import jax.numpy as jnp
from jax import lax
from jax.sharding import PartitionSpec as P

epsilon = 1e-05


def swiglu_grads(hidden_grad, pre_gate, pre_up):
    gate_wide = pre_gate.astype(jnp.float32)
    up_wide = pre_up.astype(jnp.float32)
    sigmoid = jax.nn.sigmoid(gate_wide)
    silu = gate_wide * sigmoid
    hidden = (silu * up_wide).astype(jnp.bfloat16)
    up_grad = (hidden_grad * silu).astype(jnp.bfloat16)
    gate_grad = (hidden_grad * up_wide * sigmoid * (1.0 + gate_wide * (1.0 - sigmoid))).astype(
        jnp.bfloat16
    )
    return (hidden, gate_grad, up_grad)


def row_gather(x):
    rows = lax.axis_size("row")
    copies = jnp.broadcast_to(x[None], (rows,) + x.shape)
    got = lax.all_to_all(copies, "row", split_axis=0, concat_axis=0, tiled=True)
    return got.reshape((rows * x.shape[0],) + x.shape[1:])


def local(tokens, gain, grad_out, pre_gate, pre_up, gate_weight, up_weight, down_weight):
    cols = lax.axis_size("col")
    rows = lax.axis_size("row")
    tokens_wide = tokens.astype(jnp.float32)
    inverse_rms = lax.rsqrt(jnp.mean(tokens_wide * tokens_wide, axis=1, keepdims=True) + epsilon)
    normed = tokens_wide * inverse_rms
    tile = gate_weight.shape[0]
    gain_tile = lax.dynamic_slice_in_dim(gain, lax.axis_index("col") * tile, tile)
    grid_normed = lax.all_to_all(normed, "col", split_axis=1, concat_axis=0, tiled=True)
    grid_grad = lax.all_to_all(grad_out, "col", split_axis=1, concat_axis=0, tiled=True)
    all_grad = row_gather(grid_grad)
    partial_grad = jnp.einsum(
        "td,fd->tf", all_grad, down_weight, preferred_element_type=jnp.float32
    )
    terms = partial_grad.astype(jnp.bfloat16).reshape(cols, -1, partial_grad.shape[1])
    terms = lax.all_to_all(terms, "col", split_axis=0, concat_axis=0, tiled=True)
    block_grad = jnp.sum(terms.astype(jnp.float32), axis=0)
    hidden_block, gate_block, up_block = swiglu_grads(block_grad, pre_gate, pre_up)
    gate_piece = lax.all_gather(gate_block, "col", axis=0, tiled=True)
    up_piece = lax.all_gather(up_block, "col", axis=0, tiled=True)
    hidden_piece = lax.all_gather(hidden_block, "col", axis=0, tiled=True)
    all_normed = row_gather(grid_normed)
    all_input = (all_normed * gain_tile).astype(jnp.bfloat16)
    new_rows = jnp.einsum("tf,df->td", gate_piece, gate_weight, preferred_element_type=jnp.float32)
    new_rows = new_rows + jnp.einsum(
        "tf,df->td", up_piece, up_weight, preferred_element_type=jnp.float32
    )
    gain_part = jnp.sum(new_rows * all_normed, axis=0)
    tokens_all = new_rows.shape[0]
    blocks = new_rows.reshape(rows, tokens_all // rows, tile)
    extra = jnp.zeros((rows, 8, tile), jnp.float32).at[:, 0, :].set(gain_part)
    sent = jnp.concatenate([blocks, extra], axis=1)
    got = lax.all_to_all(sent, "row", split_axis=0, concat_axis=0, tiled=True)
    summed = jnp.sum(got, axis=0)
    grid_back = summed[: tokens_all // rows]
    gain_tile_grad = summed[tokens_all // rows]
    per_col = grid_back.reshape(cols, -1, tile)
    mine = per_col.shape[1]
    sent2 = jnp.concatenate(
        [per_col, jnp.broadcast_to(gain_tile_grad[None, None, :], (cols, 1, tile))], axis=1
    )
    got2 = lax.all_to_all(sent2, "col", split_axis=0, concat_axis=0, tiled=True)
    normed_grad = got2[:, :mine, :].transpose(1, 0, 2).reshape(mine, cols * tile)
    grad_gain = got2[:, mine, :].reshape(cols * tile)
    gate_total = jnp.einsum("td,tf->df", all_input, gate_piece, preferred_element_type=jnp.float32)
    up_total = jnp.einsum("td,tf->df", all_input, up_piece, preferred_element_type=jnp.float32)
    down_total = jnp.einsum("tf,td->fd", hidden_piece, all_grad, preferred_element_type=jnp.float32)
    scaled_grad = normed_grad * gain
    inner = jnp.mean(scaled_grad * normed, axis=1, keepdims=True)
    grad_tokens = (
        grad_out.astype(jnp.float32) + inverse_rms * (scaled_grad - normed * inner)
    ).astype(jnp.bfloat16)
    return (
        grad_tokens,
        grad_gain,
        gate_total.astype(jnp.bfloat16),
        up_total.astype(jnp.bfloat16),
        down_total.astype(jnp.bfloat16),
    )


def solution(mesh):
    in_specs = (
        P(("row", "col"), None),
        P(),
        P(("row", "col"), None),
        P("col", "row"),
        P("col", "row"),
        P("col", "row"),
        P("col", "row"),
        P("row", "col"),
    )
    out_specs = (P(("row", "col"), None), P(), P("col", "row"), P("col", "row"), P("row", "col"))
    return jax.shard_map(local, mesh=mesh, in_specs=in_specs, out_specs=out_specs, check_vma=False)
```

```python
import jax
import jax.numpy as jnp
from jax import lax
from jax.sharding import PartitionSpec as P

epsilon = 1e-05


def swiglu_grads(hidden_grad, pre_gate, pre_up):
    gate_wide = pre_gate.astype(jnp.float32)
    up_wide = pre_up.astype(jnp.float32)
    sigmoid = jax.nn.sigmoid(gate_wide)
    silu = gate_wide * sigmoid
    hidden = (silu * up_wide).astype(jnp.bfloat16)
    up_grad = (hidden_grad * silu).astype(jnp.bfloat16)
    gate_grad = (hidden_grad * up_wide * sigmoid * (1.0 + gate_wide * (1.0 - sigmoid))).astype(
        jnp.bfloat16
    )
    return (hidden, gate_grad, up_grad)


def row_gather(x):
    rows = lax.axis_size("row")
    copies = jnp.broadcast_to(x[None], (rows,) + x.shape)
    got = lax.all_to_all(copies, "row", split_axis=0, concat_axis=0, tiled=True)
    return got.reshape((rows * x.shape[0],) + x.shape[1:])


def local(tokens, gain, grad_out, pre_gate, pre_up, gate_weight, up_weight, down_weight):
    cols = lax.axis_size("col")
    rows = lax.axis_size("row")
    tokens_wide = tokens.astype(jnp.float32)
    inverse_rms = lax.rsqrt(jnp.mean(tokens_wide * tokens_wide, axis=1, keepdims=True) + epsilon)
    normed = tokens_wide * inverse_rms
    tile = gate_weight.shape[0]
    gain_tile = lax.dynamic_slice_in_dim(gain, lax.axis_index("col") * tile, tile)
    mine_rows = tokens.shape[0]
    lanes = 128
    packed = jnp.concatenate(
        [
            grad_out.astype(jnp.float32).reshape(mine_rows, cols, tile),
            tokens_wide.reshape(mine_rows, cols, tile),
            jnp.broadcast_to(inverse_rms[:, :, None], (mine_rows, cols, lanes)),
        ],
        axis=2,
    )
    grid = lax.all_to_all(packed, "col", split_axis=1, concat_axis=0, tiled=True)
    grid = grid.reshape(cols * mine_rows, 2 * tile + lanes)
    grid_grad = grid[:, :tile].astype(jnp.bfloat16)
    grid_tokens = grid[:, tile : 2 * tile].astype(jnp.bfloat16)
    grid_scale = grid[:, 2 * tile : 2 * tile + 1].reshape(1, cols * mine_rows)
    all_grad = row_gather(grid_grad)
    partial_grad = jnp.einsum(
        "td,fd->tf", all_grad, down_weight, preferred_element_type=jnp.float32
    )
    block_grad = lax.psum_scatter(partial_grad, "col", scatter_dimension=0, tiled=True)
    hidden_block, gate_block, up_block = swiglu_grads(block_grad, pre_gate, pre_up)
    gate_piece = lax.all_gather(gate_block, "col", axis=0, tiled=True)
    up_piece = lax.all_gather(up_block, "col", axis=0, tiled=True)
    hidden_piece = lax.all_gather(hidden_block, "col", axis=0, tiled=True)
    all_tokens = row_gather(grid_tokens).astype(jnp.float32)
    all_scale = row_gather(grid_scale).reshape(-1, 1)
    all_normed = all_tokens * all_scale
    all_input = (all_normed * gain_tile).astype(jnp.bfloat16)
    new_rows = jnp.einsum("tf,df->td", gate_piece, gate_weight, preferred_element_type=jnp.float32)
    new_rows = new_rows + jnp.einsum(
        "tf,df->td", up_piece, up_weight, preferred_element_type=jnp.float32
    )
    gain_part = jnp.sum(new_rows * all_normed, axis=0)
    tokens_all = new_rows.shape[0]
    blocks = new_rows.reshape(rows, tokens_all // rows, tile)
    extra = jnp.zeros((rows, 8, tile), jnp.float32).at[:, 0, :].set(gain_part)
    sent = jnp.concatenate([blocks, extra], axis=1)
    got = lax.all_to_all(sent, "row", split_axis=0, concat_axis=0, tiled=True)
    summed = jnp.sum(got, axis=0)
    grid_back = summed[: tokens_all // rows]
    gain_tile_grad = summed[tokens_all // rows]
    per_col = grid_back.reshape(cols, -1, tile)
    mine = per_col.shape[1]
    sent2 = jnp.concatenate(
        [per_col, jnp.broadcast_to(gain_tile_grad[None, None, :], (cols, 1, tile))], axis=1
    )
    got2 = lax.all_to_all(sent2, "col", split_axis=0, concat_axis=0, tiled=True)
    normed_grad = got2[:, :mine, :].transpose(1, 0, 2).reshape(mine, cols * tile)
    grad_gain = got2[:, mine, :].reshape(cols * tile)
    gate_total = jnp.einsum("td,tf->df", all_input, gate_piece, preferred_element_type=jnp.float32)
    up_total = jnp.einsum("td,tf->df", all_input, up_piece, preferred_element_type=jnp.float32)
    down_total = jnp.einsum("tf,td->fd", hidden_piece, all_grad, preferred_element_type=jnp.float32)
    scaled_grad = normed_grad * gain
    inner = jnp.mean(scaled_grad * normed, axis=1, keepdims=True)
    grad_tokens = (
        grad_out.astype(jnp.float32) + inverse_rms * (scaled_grad - normed * inner)
    ).astype(jnp.bfloat16)
    return (
        grad_tokens,
        grad_gain,
        gate_total.astype(jnp.bfloat16),
        up_total.astype(jnp.bfloat16),
        down_total.astype(jnp.bfloat16),
    )


def solution(mesh):
    in_specs = (
        P(("row", "col"), None),
        P(),
        P(("row", "col"), None),
        P("col", "row"),
        P("col", "row"),
        P("col", "row"),
        P("col", "row"),
        P("row", "col"),
    )
    out_specs = (P(("row", "col"), None), P(), P("col", "row"), P("col", "row"), P("row", "col"))
    return jax.shard_map(local, mesh=mesh, in_specs=in_specs, out_specs=out_specs, check_vma=False)
```

```python
import jax
import jax.numpy as jnp
from jax import lax
from jax.sharding import PartitionSpec as P

epsilon = 1e-05


def swiglu_grads(hidden_grad, pre_gate, pre_up):
    gate_wide = pre_gate.astype(jnp.float32)
    up_wide = pre_up.astype(jnp.float32)
    sigmoid = jax.nn.sigmoid(gate_wide)
    silu = gate_wide * sigmoid
    hidden = (silu * up_wide).astype(jnp.bfloat16)
    up_grad = (hidden_grad * silu).astype(jnp.bfloat16)
    gate_grad = (hidden_grad * up_wide * sigmoid * (1.0 + gate_wide * (1.0 - sigmoid))).astype(
        jnp.bfloat16
    )
    return (hidden, gate_grad, up_grad)


def row_gather(x):
    rows = lax.axis_size("row")
    copies = jnp.broadcast_to(x[None], (rows,) + x.shape)
    got = lax.all_to_all(copies, "row", split_axis=0, concat_axis=0, tiled=True)
    return got.reshape((rows * x.shape[0],) + x.shape[1:])


def local(tokens, gain, grad_out, pre_gate, pre_up, gate_weight, up_weight, down_weight):
    cols = lax.axis_size("col")
    rows = lax.axis_size("row")
    tokens_wide = tokens.astype(jnp.float32)
    inverse_rms = lax.rsqrt(jnp.mean(tokens_wide * tokens_wide, axis=1, keepdims=True) + epsilon)
    normed = tokens_wide * inverse_rms
    tile = gate_weight.shape[0]
    gain_tile = lax.dynamic_slice_in_dim(gain, lax.axis_index("col") * tile, tile)
    mine_rows = tokens.shape[0]
    lanes = 128
    grid_grad = lax.all_to_all(grad_out, "col", split_axis=1, concat_axis=0, tiled=True)
    packed = jnp.concatenate(
        [
            tokens_wide.reshape(mine_rows, cols, tile),
            jnp.broadcast_to(inverse_rms[:, :, None], (mine_rows, cols, lanes)),
        ],
        axis=2,
    )
    grid = lax.all_to_all(packed, "col", split_axis=1, concat_axis=0, tiled=True)
    grid = grid.reshape(cols * mine_rows, tile + lanes)
    grid_tokens = grid[:, :tile].astype(jnp.bfloat16)
    grid_scale = grid[:, tile : tile + 1].reshape(1, cols * mine_rows)
    all_grad = row_gather(grid_grad)
    partial_grad = jnp.einsum(
        "td,fd->tf", all_grad, down_weight, preferred_element_type=jnp.float32
    )
    block_grad = lax.psum_scatter(partial_grad, "col", scatter_dimension=0, tiled=True)
    hidden_block, gate_block, up_block = swiglu_grads(block_grad, pre_gate, pre_up)
    gate_piece = lax.all_gather(gate_block, "col", axis=0, tiled=True)
    up_piece = lax.all_gather(up_block, "col", axis=0, tiled=True)
    hidden_piece = lax.all_gather(hidden_block, "col", axis=0, tiled=True)
    all_tokens = row_gather(grid_tokens).astype(jnp.float32)
    all_scale = row_gather(grid_scale).reshape(-1, 1)
    all_normed = all_tokens * all_scale
    all_input = (all_normed * gain_tile).astype(jnp.bfloat16)
    new_rows = jnp.einsum("tf,df->td", gate_piece, gate_weight, preferred_element_type=jnp.float32)
    new_rows = new_rows + jnp.einsum(
        "tf,df->td", up_piece, up_weight, preferred_element_type=jnp.float32
    )
    gain_part = jnp.sum(new_rows * all_normed, axis=0)
    tokens_all = new_rows.shape[0]
    blocks = new_rows.astype(jnp.bfloat16).reshape(rows, tokens_all // rows, tile)
    gain_high = gain_part.astype(jnp.bfloat16)
    gain_low = (gain_part - gain_high.astype(jnp.float32)).astype(jnp.bfloat16)
    extra = jnp.zeros((rows, 8, tile), jnp.bfloat16)
    extra = extra.at[:, 0, :].set(gain_high).at[:, 1, :].set(gain_low)
    sent = jnp.concatenate([blocks, extra], axis=1)
    got = lax.all_to_all(sent, "row", split_axis=0, concat_axis=0, tiled=True)
    summed = jnp.sum(got.astype(jnp.float32), axis=0)
    grid_back = summed[: tokens_all // rows]
    gain_tile_grad = summed[tokens_all // rows] + summed[tokens_all // rows + 1]
    per_col = grid_back.reshape(cols, -1, tile)
    mine = per_col.shape[1]
    sent2 = jnp.concatenate(
        [per_col, jnp.broadcast_to(gain_tile_grad[None, None, :], (cols, 1, tile))], axis=1
    )
    got2 = lax.all_to_all(sent2, "col", split_axis=0, concat_axis=0, tiled=True)
    normed_grad = got2[:, :mine, :].transpose(1, 0, 2).reshape(mine, cols * tile)
    grad_gain = got2[:, mine, :].reshape(cols * tile)
    gate_total = jnp.einsum("td,tf->df", all_input, gate_piece, preferred_element_type=jnp.float32)
    up_total = jnp.einsum("td,tf->df", all_input, up_piece, preferred_element_type=jnp.float32)
    down_total = jnp.einsum("tf,td->fd", hidden_piece, all_grad, preferred_element_type=jnp.float32)
    scaled_grad = normed_grad * gain
    inner = jnp.mean(scaled_grad * normed, axis=1, keepdims=True)
    grad_tokens = (
        grad_out.astype(jnp.float32) + inverse_rms * (scaled_grad - normed * inner)
    ).astype(jnp.bfloat16)
    return (
        grad_tokens,
        grad_gain,
        gate_total.astype(jnp.bfloat16),
        up_total.astype(jnp.bfloat16),
        down_total.astype(jnp.bfloat16),
    )


def solution(mesh):
    in_specs = (
        P(("row", "col"), None),
        P(),
        P(("row", "col"), None),
        P("col", "row"),
        P("col", "row"),
        P("col", "row"),
        P("col", "row"),
        P("row", "col"),
    )
    out_specs = (P(("row", "col"), None), P(), P("col", "row"), P("col", "row"), P("row", "col"))
    return jax.shard_map(local, mesh=mesh, in_specs=in_specs, out_specs=out_specs, check_vma=False)
```

```python
import jax
import jax.numpy as jnp
from jax import lax
from jax.sharding import PartitionSpec as P

epsilon = 1e-05


def swiglu_grads(hidden_grad, pre_gate, pre_up):
    gate_wide = pre_gate.astype(jnp.float32)
    up_wide = pre_up.astype(jnp.float32)
    sigmoid = jax.nn.sigmoid(gate_wide)
    silu = gate_wide * sigmoid
    hidden = (silu * up_wide).astype(jnp.bfloat16)
    up_grad = (hidden_grad * silu).astype(jnp.bfloat16)
    gate_grad = (hidden_grad * up_wide * sigmoid * (1.0 + gate_wide * (1.0 - sigmoid))).astype(
        jnp.bfloat16
    )
    return (hidden, gate_grad, up_grad)


def row_gather(x):
    rows = lax.axis_size("row")
    copies = jnp.broadcast_to(x[None], (rows,) + x.shape)
    got = lax.all_to_all(copies, "row", split_axis=0, concat_axis=0, tiled=True)
    return got.reshape((rows * x.shape[0],) + x.shape[1:])


def local(tokens, gain, grad_out, pre_gate, pre_up, gate_weight, up_weight, down_weight):
    cols = lax.axis_size("col")
    rows = lax.axis_size("row")
    tokens_wide = tokens.astype(jnp.float32)
    inverse_rms = lax.rsqrt(jnp.mean(tokens_wide * tokens_wide, axis=1, keepdims=True) + epsilon)
    normed = tokens_wide * inverse_rms
    tile = gate_weight.shape[0]
    gain_tile = lax.dynamic_slice_in_dim(gain, lax.axis_index("col") * tile, tile)
    mine_rows = tokens.shape[0]
    lanes = 128
    grid_grad = lax.all_to_all(grad_out, "col", split_axis=1, concat_axis=0, tiled=True)
    packed = jnp.concatenate(
        [
            tokens_wide.reshape(mine_rows, cols, tile),
            jnp.broadcast_to(inverse_rms[:, :, None], (mine_rows, cols, lanes)),
        ],
        axis=2,
    )
    grid = lax.all_to_all(packed, "col", split_axis=1, concat_axis=0, tiled=True)
    grid = grid.reshape(cols * mine_rows, tile + lanes)
    grid_tokens = grid[:, :tile].astype(jnp.bfloat16)
    grid_scale = grid[:, tile : tile + 1].reshape(1, cols * mine_rows)
    all_grad = row_gather(grid_grad)
    hidden_block = swiglu_grads(jnp.zeros(pre_gate.shape, jnp.float32), pre_gate, pre_up)[0]
    hidden_piece = lax.all_gather(hidden_block, "col", axis=0, tiled=True)
    partial_grad = jnp.einsum(
        "td,fd->tf", all_grad, down_weight, preferred_element_type=jnp.float32
    )
    hidden_piece, partial_grad = lax.optimization_barrier((hidden_piece, partial_grad))
    block_grad = lax.psum_scatter(partial_grad, "col", scatter_dimension=0, tiled=True)
    _, gate_block, up_block = swiglu_grads(block_grad, pre_gate, pre_up)
    gate_piece = lax.all_gather(gate_block, "col", axis=0, tiled=True)
    up_piece = lax.all_gather(up_block, "col", axis=0, tiled=True)
    all_tokens = row_gather(grid_tokens).astype(jnp.float32)
    all_scale = row_gather(grid_scale).reshape(-1, 1)
    all_normed = all_tokens * all_scale
    all_input = (all_normed * gain_tile).astype(jnp.bfloat16)
    new_rows = jnp.einsum("tf,df->td", gate_piece, gate_weight, preferred_element_type=jnp.float32)
    new_rows = new_rows + jnp.einsum(
        "tf,df->td", up_piece, up_weight, preferred_element_type=jnp.float32
    )
    gain_part = jnp.sum(new_rows * all_normed, axis=0)
    tokens_all = new_rows.shape[0]
    blocks = new_rows.astype(jnp.bfloat16).reshape(rows, tokens_all // rows, tile)
    gain_high = gain_part.astype(jnp.bfloat16)
    gain_low = (gain_part - gain_high.astype(jnp.float32)).astype(jnp.bfloat16)
    extra = jnp.zeros((rows, 8, tile), jnp.bfloat16)
    extra = extra.at[:, 0, :].set(gain_high).at[:, 1, :].set(gain_low)
    sent = jnp.concatenate([blocks, extra], axis=1)
    got = lax.all_to_all(sent, "row", split_axis=0, concat_axis=0, tiled=True)
    summed = jnp.sum(got.astype(jnp.float32), axis=0)
    grid_back = summed[: tokens_all // rows]
    gain_tile_grad = summed[tokens_all // rows] + summed[tokens_all // rows + 1]
    per_col = grid_back.reshape(cols, -1, tile)
    mine = per_col.shape[1]
    sent2 = jnp.concatenate(
        [per_col, jnp.broadcast_to(gain_tile_grad[None, None, :], (cols, 1, tile))], axis=1
    )
    got2 = lax.all_to_all(sent2, "col", split_axis=0, concat_axis=0, tiled=True)
    normed_grad = got2[:, :mine, :].transpose(1, 0, 2).reshape(mine, cols * tile)
    grad_gain = got2[:, mine, :].reshape(cols * tile)
    gate_total = jnp.einsum("td,tf->df", all_input, gate_piece, preferred_element_type=jnp.float32)
    up_total = jnp.einsum("td,tf->df", all_input, up_piece, preferred_element_type=jnp.float32)
    down_total = jnp.einsum("tf,td->fd", hidden_piece, all_grad, preferred_element_type=jnp.float32)
    scaled_grad = normed_grad * gain
    inner = jnp.mean(scaled_grad * normed, axis=1, keepdims=True)
    grad_tokens = (
        grad_out.astype(jnp.float32) + inverse_rms * (scaled_grad - normed * inner)
    ).astype(jnp.bfloat16)
    return (
        grad_tokens,
        grad_gain,
        gate_total.astype(jnp.bfloat16),
        up_total.astype(jnp.bfloat16),
        down_total.astype(jnp.bfloat16),
    )


def solution(mesh):
    in_specs = (
        P(("row", "col"), None),
        P(),
        P(("row", "col"), None),
        P("col", "row"),
        P("col", "row"),
        P("col", "row"),
        P("col", "row"),
        P("row", "col"),
    )
    out_specs = (P(("row", "col"), None), P(), P("col", "row"), P("col", "row"), P("row", "col"))
    return jax.shard_map(local, mesh=mesh, in_specs=in_specs, out_specs=out_specs, check_vma=False)
```

```python
import jax
import jax.numpy as jnp
from jax import lax
from jax.sharding import PartitionSpec as P

epsilon = 1e-05


def swiglu_grads(hidden_grad, pre_gate, pre_up):
    gate_wide = pre_gate.astype(jnp.float32)
    up_wide = pre_up.astype(jnp.float32)
    sigmoid = jax.nn.sigmoid(gate_wide)
    silu = gate_wide * sigmoid
    hidden = (silu * up_wide).astype(jnp.bfloat16)
    up_grad = (hidden_grad * silu).astype(jnp.bfloat16)
    gate_grad = (hidden_grad * up_wide * sigmoid * (1.0 + gate_wide * (1.0 - sigmoid))).astype(
        jnp.bfloat16
    )
    return (hidden, gate_grad, up_grad)


def row_gather(x):
    rows = lax.axis_size("row")
    copies = jnp.broadcast_to(x[None], (rows,) + x.shape)
    got = lax.all_to_all(copies, "row", split_axis=0, concat_axis=0, tiled=True)
    return got.reshape((rows * x.shape[0],) + x.shape[1:])


def local(tokens, gain, grad_out, pre_gate, pre_up, gate_weight, up_weight, down_weight):
    cols = lax.axis_size("col")
    rows = lax.axis_size("row")
    tokens_wide = tokens.astype(jnp.float32)
    inverse_rms = lax.rsqrt(jnp.mean(tokens_wide * tokens_wide, axis=1, keepdims=True) + epsilon)
    normed = tokens_wide * inverse_rms
    tile = gate_weight.shape[0]
    gain_tile = lax.dynamic_slice_in_dim(gain, lax.axis_index("col") * tile, tile)
    mine_rows = tokens.shape[0]
    lanes = 128
    grid_grad = lax.all_to_all(grad_out, "col", split_axis=1, concat_axis=0, tiled=True)
    packed = jnp.concatenate(
        [
            tokens_wide.reshape(mine_rows, cols, tile),
            jnp.broadcast_to(inverse_rms[:, :, None], (mine_rows, cols, lanes)),
        ],
        axis=2,
    )
    grid = lax.all_to_all(packed, "col", split_axis=1, concat_axis=0, tiled=True)
    grid = grid.reshape(cols * mine_rows, tile + lanes)
    grid_tokens = grid[:, :tile].astype(jnp.bfloat16)
    grid_scale = grid[:, tile : tile + 1].reshape(1, cols * mine_rows)
    all_grad = row_gather(grid_grad)
    hidden_block = swiglu_grads(jnp.zeros(pre_gate.shape, jnp.float32), pre_gate, pre_up)[0]
    hidden_piece = lax.all_gather(hidden_block, "col", axis=0, tiled=True)
    partial_grad = jnp.einsum(
        "td,fd->tf", all_grad, down_weight, preferred_element_type=jnp.float32
    )
    hidden_piece, partial_grad = lax.optimization_barrier((hidden_piece, partial_grad))
    block_grad = lax.psum_scatter(partial_grad, "col", scatter_dimension=0, tiled=True)
    down_total = jnp.einsum("tf,td->fd", hidden_piece, all_grad, preferred_element_type=jnp.float32)
    down_total, block_grad = lax.optimization_barrier((down_total, block_grad))
    _, gate_block, up_block = swiglu_grads(block_grad, pre_gate, pre_up)
    all_tokens = row_gather(grid_tokens).astype(jnp.float32)
    all_scale = row_gather(grid_scale).reshape(-1, 1)
    all_normed = all_tokens * all_scale
    all_input = (all_normed * gain_tile).astype(jnp.bfloat16)
    gate_piece = lax.all_gather(gate_block, "col", axis=0, tiled=True)
    up_piece = lax.all_gather(up_block, "col", axis=0, tiled=True)
    gate_total = jnp.einsum("td,tf->df", all_input, gate_piece, preferred_element_type=jnp.float32)
    gate_total, up_piece = lax.optimization_barrier((gate_total, up_piece))
    new_rows = jnp.einsum("tf,df->td", gate_piece, gate_weight, preferred_element_type=jnp.float32)
    new_rows = new_rows + jnp.einsum(
        "tf,df->td", up_piece, up_weight, preferred_element_type=jnp.float32
    )
    gain_part = jnp.sum(new_rows * all_normed, axis=0)
    tokens_all = new_rows.shape[0]
    blocks = new_rows.astype(jnp.bfloat16).reshape(rows, tokens_all // rows, tile)
    gain_high = gain_part.astype(jnp.bfloat16)
    gain_low = (gain_part - gain_high.astype(jnp.float32)).astype(jnp.bfloat16)
    extra = jnp.zeros((rows, 8, tile), jnp.bfloat16)
    extra = extra.at[:, 0, :].set(gain_high).at[:, 1, :].set(gain_low)
    sent = jnp.concatenate([blocks, extra], axis=1)
    got = lax.all_to_all(sent, "row", split_axis=0, concat_axis=0, tiled=True)
    summed = jnp.sum(got.astype(jnp.float32), axis=0)
    grid_back = summed[: tokens_all // rows]
    gain_tile_grad = summed[tokens_all // rows] + summed[tokens_all // rows + 1]
    per_col = grid_back.reshape(cols, -1, tile)
    mine = per_col.shape[1]
    sent2 = jnp.concatenate(
        [per_col, jnp.broadcast_to(gain_tile_grad[None, None, :], (cols, 1, tile))], axis=1
    )
    got2 = lax.all_to_all(sent2, "col", split_axis=0, concat_axis=0, tiled=True)
    normed_grad = got2[:, :mine, :].transpose(1, 0, 2).reshape(mine, cols * tile)
    grad_gain = got2[:, mine, :].reshape(cols * tile)
    up_total = jnp.einsum("td,tf->df", all_input, up_piece, preferred_element_type=jnp.float32)
    scaled_grad = normed_grad * gain
    inner = jnp.mean(scaled_grad * normed, axis=1, keepdims=True)
    grad_tokens = (
        grad_out.astype(jnp.float32) + inverse_rms * (scaled_grad - normed * inner)
    ).astype(jnp.bfloat16)
    return (
        grad_tokens,
        grad_gain,
        gate_total.astype(jnp.bfloat16),
        up_total.astype(jnp.bfloat16),
        down_total.astype(jnp.bfloat16),
    )


def solution(mesh):
    in_specs = (
        P(("row", "col"), None),
        P(),
        P(("row", "col"), None),
        P("col", "row"),
        P("col", "row"),
        P("col", "row"),
        P("col", "row"),
        P("row", "col"),
    )
    out_specs = (P(("row", "col"), None), P(), P("col", "row"), P("col", "row"), P("row", "col"))
    return jax.shard_map(local, mesh=mesh, in_specs=in_specs, out_specs=out_specs, check_vma=False)
```

```python
import jax
import jax.numpy as jnp
from jax import lax
from jax.sharding import PartitionSpec as P

epsilon = 1e-05


def swiglu_grads(hidden_grad, pre_gate, pre_up):
    gate_wide = pre_gate.astype(jnp.float32)
    up_wide = pre_up.astype(jnp.float32)
    sigmoid = jax.nn.sigmoid(gate_wide)
    silu = gate_wide * sigmoid
    hidden = (silu * up_wide).astype(jnp.bfloat16)
    up_grad = (hidden_grad * silu).astype(jnp.bfloat16)
    gate_grad = (hidden_grad * up_wide * sigmoid * (1.0 + gate_wide * (1.0 - sigmoid))).astype(
        jnp.bfloat16
    )
    return (hidden, gate_grad, up_grad)


def row_gather(x):
    rows = lax.axis_size("row")
    copies = jnp.broadcast_to(x[None], (rows,) + x.shape)
    got = lax.all_to_all(copies, "row", split_axis=0, concat_axis=0, tiled=True)
    return got.reshape((rows * x.shape[0],) + x.shape[1:])


def local(tokens, gain, grad_out, pre_gate, pre_up, gate_weight, up_weight, down_weight):
    cols = lax.axis_size("col")
    rows = lax.axis_size("row")
    tokens_wide = tokens.astype(jnp.float32)
    inverse_rms = lax.rsqrt(jnp.mean(tokens_wide * tokens_wide, axis=1, keepdims=True) + epsilon)
    normed = tokens_wide * inverse_rms
    tile = gate_weight.shape[0]
    gain_tile = lax.dynamic_slice_in_dim(gain, lax.axis_index("col") * tile, tile)
    mine_rows = tokens.shape[0]
    lanes = 128
    grid_grad = lax.all_to_all(grad_out, "col", split_axis=1, concat_axis=0, tiled=True)
    packed = jnp.concatenate(
        [
            tokens_wide.reshape(mine_rows, cols, tile),
            jnp.broadcast_to(inverse_rms[:, :, None], (mine_rows, cols, lanes)),
        ],
        axis=2,
    )
    grid = lax.all_to_all(packed, "col", split_axis=1, concat_axis=0, tiled=True)
    grid = grid.reshape(cols * mine_rows, tile + lanes)
    grid_tokens = grid[:, :tile].astype(jnp.bfloat16)
    grid_scale = grid[:, tile : tile + 1].reshape(1, cols * mine_rows)
    all_grad = row_gather(grid_grad)
    hidden_block = swiglu_grads(jnp.zeros(pre_gate.shape, jnp.float32), pre_gate, pre_up)[0]
    split = (hidden_block.shape[1] // 256) * 128
    hidden_piece = lax.all_gather(hidden_block[:, :split], "col", axis=0, tiled=True)
    partial_grad = jnp.einsum(
        "td,fd->tf", all_grad, down_weight, preferred_element_type=jnp.float32
    )
    hidden_piece, partial_grad = lax.optimization_barrier((hidden_piece, partial_grad))
    block_grad = lax.psum_scatter(partial_grad, "col", scatter_dimension=0, tiled=True)
    down_total = jnp.einsum("tf,td->fd", hidden_piece, all_grad, preferred_element_type=jnp.float32)
    down_total, block_grad = lax.optimization_barrier((down_total, block_grad))
    _, gate_block, up_block = swiglu_grads(block_grad, pre_gate, pre_up)
    all_tokens = row_gather(grid_tokens).astype(jnp.float32)
    all_scale = row_gather(grid_scale).reshape(-1, 1)
    all_normed = all_tokens * all_scale
    all_input = (all_normed * gain_tile).astype(jnp.bfloat16)
    gate_piece = lax.all_gather(gate_block, "col", axis=0, tiled=True)
    up_piece = lax.all_gather(up_block, "col", axis=0, tiled=True)
    gate_total = jnp.einsum("td,tf->df", all_input, gate_piece, preferred_element_type=jnp.float32)
    gate_total, up_piece = lax.optimization_barrier((gate_total, up_piece))
    late_block, up_piece = lax.optimization_barrier((hidden_block[:, split:], up_piece))
    late_piece = lax.all_gather(late_block, "col", axis=0, tiled=True)
    new_rows = jnp.einsum("tf,df->td", gate_piece, gate_weight, preferred_element_type=jnp.float32)
    new_rows = new_rows + jnp.einsum(
        "tf,df->td", up_piece, up_weight, preferred_element_type=jnp.float32
    )
    gain_part = jnp.sum(new_rows * all_normed, axis=0)
    tokens_all = new_rows.shape[0]
    blocks = new_rows.astype(jnp.bfloat16).reshape(rows, tokens_all // rows, tile)
    gain_high = gain_part.astype(jnp.bfloat16)
    gain_low = (gain_part - gain_high.astype(jnp.float32)).astype(jnp.bfloat16)
    extra = jnp.zeros((rows, 8, tile), jnp.bfloat16)
    extra = extra.at[:, 0, :].set(gain_high).at[:, 1, :].set(gain_low)
    sent = jnp.concatenate([blocks, extra], axis=1)
    got = lax.all_to_all(sent, "row", split_axis=0, concat_axis=0, tiled=True)
    summed = jnp.sum(got.astype(jnp.float32), axis=0)
    grid_back = summed[: tokens_all // rows]
    gain_tile_grad = summed[tokens_all // rows] + summed[tokens_all // rows + 1]
    per_col = grid_back.reshape(cols, -1, tile)
    mine = per_col.shape[1]
    sent2 = jnp.concatenate(
        [per_col, jnp.broadcast_to(gain_tile_grad[None, None, :], (cols, 1, tile))], axis=1
    )
    got2 = lax.all_to_all(sent2, "col", split_axis=0, concat_axis=0, tiled=True)
    normed_grad = got2[:, :mine, :].transpose(1, 0, 2).reshape(mine, cols * tile)
    grad_gain = got2[:, mine, :].reshape(cols * tile)
    up_total = jnp.einsum("td,tf->df", all_input, up_piece, preferred_element_type=jnp.float32)
    down_late = jnp.einsum("tf,td->fd", late_piece, all_grad, preferred_element_type=jnp.float32)
    scaled_grad = normed_grad * gain
    inner = jnp.mean(scaled_grad * normed, axis=1, keepdims=True)
    grad_tokens = (
        grad_out.astype(jnp.float32) + inverse_rms * (scaled_grad - normed * inner)
    ).astype(jnp.bfloat16)
    return (
        grad_tokens,
        grad_gain,
        gate_total.astype(jnp.bfloat16),
        up_total.astype(jnp.bfloat16),
        jnp.concatenate([down_total, down_late], axis=0).astype(jnp.bfloat16),
    )


def solution(mesh):
    in_specs = (
        P(("row", "col"), None),
        P(),
        P(("row", "col"), None),
        P("col", "row"),
        P("col", "row"),
        P("col", "row"),
        P("col", "row"),
        P("row", "col"),
    )
    out_specs = (P(("row", "col"), None), P(), P("col", "row"), P("col", "row"), P("row", "col"))
    return jax.shard_map(local, mesh=mesh, in_specs=in_specs, out_specs=out_specs, check_vma=False)
```

```python
import jax
import jax.numpy as jnp
from jax import lax
from jax.sharding import PartitionSpec as P

epsilon = 1e-05


def swiglu_grads(hidden_grad, pre_gate, pre_up):
    gate_wide = pre_gate.astype(jnp.float32)
    up_wide = pre_up.astype(jnp.float32)
    sigmoid = jax.nn.sigmoid(gate_wide)
    silu = gate_wide * sigmoid
    hidden = (silu * up_wide).astype(jnp.bfloat16)
    up_grad = (hidden_grad * silu).astype(jnp.bfloat16)
    gate_grad = (hidden_grad * up_wide * sigmoid * (1.0 + gate_wide * (1.0 - sigmoid))).astype(
        jnp.bfloat16
    )
    return (hidden, gate_grad, up_grad)


def row_gather(x):
    rows = lax.axis_size("row")
    copies = jnp.broadcast_to(x[None], (rows,) + x.shape)
    got = lax.all_to_all(copies, "row", split_axis=0, concat_axis=0, tiled=True)
    return got.reshape((rows * x.shape[0],) + x.shape[1:])


def local(tokens, gain, grad_out, pre_gate, pre_up, gate_weight, up_weight, down_weight):
    cols = lax.axis_size("col")
    rows = lax.axis_size("row")
    tokens_wide = tokens.astype(jnp.float32)
    inverse_rms = lax.rsqrt(jnp.mean(tokens_wide * tokens_wide, axis=1, keepdims=True) + epsilon)
    normed = tokens_wide * inverse_rms
    tile = gate_weight.shape[0]
    gain_tile = lax.dynamic_slice_in_dim(gain, lax.axis_index("col") * tile, tile)
    mine_rows = tokens.shape[0]
    lanes = 128
    grid_grad = lax.all_to_all(grad_out, "col", split_axis=1, concat_axis=0, tiled=True)
    packed = jnp.concatenate(
        [
            tokens_wide.reshape(mine_rows, cols, tile),
            jnp.broadcast_to(inverse_rms[:, :, None], (mine_rows, cols, lanes)),
        ],
        axis=2,
    )
    grid = lax.all_to_all(packed, "col", split_axis=1, concat_axis=0, tiled=True)
    grid = grid.reshape(cols * mine_rows, tile + lanes)
    grid_tokens = grid[:, :tile].astype(jnp.bfloat16)
    grid_scale = grid[:, tile : tile + 1].reshape(1, cols * mine_rows)
    all_grad = row_gather(grid_grad)
    hidden_block = swiglu_grads(jnp.zeros(pre_gate.shape, jnp.float32), pre_gate, pre_up)[0]
    split = (hidden_block.shape[1] // 256) * 128
    hidden_piece = lax.all_gather(hidden_block[:, :split], "col", axis=0, tiled=True)
    partial_grad = jnp.einsum(
        "td,fd->tf", all_grad, down_weight, preferred_element_type=jnp.float32
    )
    hidden_piece, partial_grad = lax.optimization_barrier((hidden_piece, partial_grad))
    block_grad = lax.psum_scatter(partial_grad, "col", scatter_dimension=0, tiled=True)
    down_total = jnp.einsum("tf,td->fd", hidden_piece, all_grad, preferred_element_type=jnp.float32)
    down_total, block_grad = lax.optimization_barrier((down_total, block_grad))
    _, gate_block, up_block = swiglu_grads(block_grad, pre_gate, pre_up)
    all_tokens = row_gather(grid_tokens).astype(jnp.float32)
    all_scale = row_gather(grid_scale).reshape(-1, 1)
    all_normed = all_tokens * all_scale
    all_input = (all_normed * gain_tile).astype(jnp.bfloat16)
    gate_piece = lax.all_gather(gate_block, "col", axis=0, tiled=True)
    up_piece = lax.all_gather(up_block, "col", axis=0, tiled=True)
    gate_total = jnp.einsum("td,tf->df", all_input, gate_piece, preferred_element_type=jnp.float32)
    gate_total, up_piece = lax.optimization_barrier((gate_total, up_piece))
    late_block, up_piece = lax.optimization_barrier((hidden_block[:, split:], up_piece))
    late_piece = lax.all_gather(late_block, "col", axis=0, tiled=True)
    new_rows = jnp.einsum("tf,df->td", gate_piece, gate_weight, preferred_element_type=jnp.float32)
    new_rows = new_rows + jnp.einsum(
        "tf,df->td", up_piece, up_weight, preferred_element_type=jnp.float32
    )
    gain_part = jnp.sum(new_rows * all_normed, axis=0)
    tokens_all = new_rows.shape[0]
    blocks = new_rows.astype(jnp.bfloat16).reshape(rows, tokens_all // rows, tile)
    gain_high = gain_part.astype(jnp.bfloat16)
    gain_low = (gain_part - gain_high.astype(jnp.float32)).astype(jnp.bfloat16)
    extra = jnp.zeros((rows, 8, tile), jnp.bfloat16)
    extra = extra.at[:, 0, :].set(gain_high).at[:, 1, :].set(gain_low)
    sent = jnp.concatenate([blocks, extra], axis=1)
    me = lax.axis_index("row")
    arrived = [lax.dynamic_index_in_dim(sent, me, 0, keepdims=False)]
    for k in range(1, rows):
        piece = lax.dynamic_index_in_dim(sent, (me + k) % rows, 0, keepdims=False)
        arrived.append(lax.ppermute(piece, "row", [(i, (i + k) % rows) for i in range(rows)]))
    ahead = jnp.stack([arrived[(-j) % rows] for j in range(rows)])
    got = jnp.roll(ahead, me, axis=0)
    summed = jnp.sum(got.astype(jnp.float32), axis=0)
    grid_back = summed[: tokens_all // rows]
    gain_tile_grad = summed[tokens_all // rows] + summed[tokens_all // rows + 1]
    per_col = grid_back.reshape(cols, -1, tile)
    mine = per_col.shape[1]
    sent2 = jnp.concatenate(
        [per_col, jnp.broadcast_to(gain_tile_grad[None, None, :], (cols, 1, tile))], axis=1
    )
    got2 = lax.all_to_all(sent2, "col", split_axis=0, concat_axis=0, tiled=True)
    normed_grad = got2[:, :mine, :].transpose(1, 0, 2).reshape(mine, cols * tile)
    grad_gain = got2[:, mine, :].reshape(cols * tile)
    up_total = jnp.einsum("td,tf->df", all_input, up_piece, preferred_element_type=jnp.float32)
    down_late = jnp.einsum("tf,td->fd", late_piece, all_grad, preferred_element_type=jnp.float32)
    scaled_grad = normed_grad * gain
    inner = jnp.mean(scaled_grad * normed, axis=1, keepdims=True)
    grad_tokens = (
        grad_out.astype(jnp.float32) + inverse_rms * (scaled_grad - normed * inner)
    ).astype(jnp.bfloat16)
    return (
        grad_tokens,
        grad_gain,
        gate_total.astype(jnp.bfloat16),
        up_total.astype(jnp.bfloat16),
        jnp.concatenate([down_total, down_late], axis=0).astype(jnp.bfloat16),
    )


def solution(mesh):
    in_specs = (
        P(("row", "col"), None),
        P(),
        P(("row", "col"), None),
        P("col", "row"),
        P("col", "row"),
        P("col", "row"),
        P("col", "row"),
        P("row", "col"),
    )
    out_specs = (P(("row", "col"), None), P(), P("col", "row"), P("col", "row"), P("row", "col"))
    return jax.shard_map(local, mesh=mesh, in_specs=in_specs, out_specs=out_specs, check_vma=False)
```

```python
import jax
import jax.numpy as jnp
from jax import lax
from jax.sharding import PartitionSpec as P

epsilon = 1e-05


def swiglu_grads(hidden_grad, pre_gate, pre_up):
    gate_wide = pre_gate.astype(jnp.float32)
    up_wide = pre_up.astype(jnp.float32)
    sigmoid = jax.nn.sigmoid(gate_wide)
    silu = gate_wide * sigmoid
    hidden = (silu * up_wide).astype(jnp.bfloat16)
    up_grad = (hidden_grad * silu).astype(jnp.bfloat16)
    gate_grad = (hidden_grad * up_wide * sigmoid * (1.0 + gate_wide * (1.0 - sigmoid))).astype(
        jnp.bfloat16
    )
    return (hidden, gate_grad, up_grad)


def row_gather(x):
    rows = lax.axis_size("row")
    copies = jnp.broadcast_to(x[None], (rows,) + x.shape)
    got = lax.all_to_all(copies, "row", split_axis=0, concat_axis=0, tiled=True)
    return got.reshape((rows * x.shape[0],) + x.shape[1:])


def local(tokens, gain, grad_out, pre_gate, pre_up, gate_weight, up_weight, down_weight):
    cols = lax.axis_size("col")
    rows = lax.axis_size("row")
    tokens_wide = tokens.astype(jnp.float32)
    inverse_rms = lax.rsqrt(jnp.mean(tokens_wide * tokens_wide, axis=1, keepdims=True) + epsilon)
    normed = tokens_wide * inverse_rms
    tile = gate_weight.shape[0]
    gain_tile = lax.dynamic_slice_in_dim(gain, lax.axis_index("col") * tile, tile)
    mine_rows = tokens.shape[0]
    lanes = 128
    grid_grad = lax.all_to_all(grad_out, "col", split_axis=1, concat_axis=0, tiled=True)
    packed = jnp.concatenate(
        [
            tokens_wide.reshape(mine_rows, cols, tile),
            jnp.broadcast_to(inverse_rms[:, :, None], (mine_rows, cols, lanes)),
        ],
        axis=2,
    )
    grid = lax.all_to_all(packed, "col", split_axis=1, concat_axis=0, tiled=True)
    grid = grid.reshape(cols * mine_rows, tile + lanes)
    grid_tokens = grid[:, :tile].astype(jnp.bfloat16)
    grid_scale = grid[:, tile : tile + 1].reshape(1, cols * mine_rows)
    all_grad = row_gather(grid_grad)
    hidden_block = swiglu_grads(jnp.zeros(pre_gate.shape, jnp.float32), pre_gate, pre_up)[0]
    split = (hidden_block.shape[1] // 448) * 128
    hidden_piece = lax.all_gather(hidden_block[:, :split], "col", axis=0, tiled=True)
    partial_grad = jnp.einsum(
        "td,fd->tf", all_grad, down_weight, preferred_element_type=jnp.float32
    )
    hidden_piece, partial_grad = lax.optimization_barrier((hidden_piece, partial_grad))
    block_grad = lax.psum_scatter(partial_grad, "col", scatter_dimension=0, tiled=True)
    down_total = jnp.einsum("tf,td->fd", hidden_piece, all_grad, preferred_element_type=jnp.float32)
    down_total, block_grad = lax.optimization_barrier((down_total, block_grad))
    _, gate_block, up_block = swiglu_grads(block_grad, pre_gate, pre_up)
    all_tokens = row_gather(grid_tokens).astype(jnp.float32)
    all_scale = row_gather(grid_scale).reshape(-1, 1)
    all_normed = all_tokens * all_scale
    all_input = (all_normed * gain_tile).astype(jnp.bfloat16)
    gate_piece = lax.all_gather(gate_block, "col", axis=0, tiled=True)
    up_piece = lax.all_gather(up_block, "col", axis=0, tiled=True)
    gate_total = jnp.einsum("td,tf->df", all_input, gate_piece, preferred_element_type=jnp.float32)
    gate_total, up_piece = lax.optimization_barrier((gate_total, up_piece))
    late_block, up_piece = lax.optimization_barrier((hidden_block[:, split:], up_piece))
    late_piece = lax.all_gather(late_block, "col", axis=0, tiled=True)
    new_rows = jnp.einsum("tf,df->td", gate_piece, gate_weight, preferred_element_type=jnp.float32)
    new_rows = new_rows + jnp.einsum(
        "tf,df->td", up_piece, up_weight, preferred_element_type=jnp.float32
    )
    gain_part = jnp.sum(new_rows * all_normed, axis=0)
    tokens_all = new_rows.shape[0]
    blocks = new_rows.astype(jnp.bfloat16).reshape(rows, tokens_all // rows, tile)
    gain_high = gain_part.astype(jnp.bfloat16)
    gain_low = (gain_part - gain_high.astype(jnp.float32)).astype(jnp.bfloat16)
    extra = jnp.zeros((rows, 8, tile), jnp.bfloat16)
    extra = extra.at[:, 0, :].set(gain_high).at[:, 1, :].set(gain_low)
    sent = jnp.concatenate([blocks, extra], axis=1)
    got = lax.all_to_all(sent, "row", split_axis=0, concat_axis=0, tiled=True)
    summed = jnp.sum(got.astype(jnp.float32), axis=0)
    grid_back = summed[: tokens_all // rows]
    gain_tile_grad = summed[tokens_all // rows] + summed[tokens_all // rows + 1]
    per_col = grid_back.reshape(cols, -1, tile)
    mine = per_col.shape[1]
    sent2 = jnp.concatenate(
        [per_col, jnp.broadcast_to(gain_tile_grad[None, None, :], (cols, 1, tile))], axis=1
    )
    got2 = lax.all_to_all(sent2, "col", split_axis=0, concat_axis=0, tiled=True)
    normed_grad = got2[:, :mine, :].transpose(1, 0, 2).reshape(mine, cols * tile)
    grad_gain = got2[:, mine, :].reshape(cols * tile)
    up_total = jnp.einsum("td,tf->df", all_input, up_piece, preferred_element_type=jnp.float32)
    down_late = jnp.einsum("tf,td->fd", late_piece, all_grad, preferred_element_type=jnp.float32)
    scaled_grad = normed_grad * gain
    inner = jnp.mean(scaled_grad * normed, axis=1, keepdims=True)
    grad_tokens = (
        grad_out.astype(jnp.float32) + inverse_rms * (scaled_grad - normed * inner)
    ).astype(jnp.bfloat16)
    return (
        grad_tokens,
        grad_gain,
        gate_total.astype(jnp.bfloat16),
        up_total.astype(jnp.bfloat16),
        jnp.concatenate([down_total, down_late], axis=0).astype(jnp.bfloat16),
    )


def solution(mesh):
    in_specs = (
        P(("row", "col"), None),
        P(),
        P(("row", "col"), None),
        P("col", "row"),
        P("col", "row"),
        P("col", "row"),
        P("col", "row"),
        P("row", "col"),
    )
    out_specs = (P(("row", "col"), None), P(), P("col", "row"), P("col", "row"), P("row", "col"))
    return jax.shard_map(local, mesh=mesh, in_specs=in_specs, out_specs=out_specs, check_vma=False)
```

```python
import jax
import jax.numpy as jnp
from jax import lax
from jax.sharding import PartitionSpec as P

epsilon = 1e-05


def swiglu_grads(hidden_grad, pre_gate, pre_up):
    gate_wide = pre_gate.astype(jnp.float32)
    up_wide = pre_up.astype(jnp.float32)
    sigmoid = jax.nn.sigmoid(gate_wide)
    silu = gate_wide * sigmoid
    hidden = (silu * up_wide).astype(jnp.bfloat16)
    up_grad = (hidden_grad * silu).astype(jnp.bfloat16)
    gate_grad = (hidden_grad * up_wide * sigmoid * (1.0 + gate_wide * (1.0 - sigmoid))).astype(
        jnp.bfloat16
    )
    return (hidden, gate_grad, up_grad)


def row_gather(x):
    rows = lax.axis_size("row")
    copies = jnp.broadcast_to(x[None], (rows,) + x.shape)
    got = lax.all_to_all(copies, "row", split_axis=0, concat_axis=0, tiled=True)
    return got.reshape((rows * x.shape[0],) + x.shape[1:])


def local(tokens, gain, grad_out, pre_gate, pre_up, gate_weight, up_weight, down_weight):
    cols = lax.axis_size("col")
    rows = lax.axis_size("row")
    tokens_wide = tokens.astype(jnp.float32)
    inverse_rms = lax.rsqrt(jnp.mean(tokens_wide * tokens_wide, axis=1, keepdims=True) + epsilon)
    normed = tokens_wide * inverse_rms
    tile = gate_weight.shape[0]
    gain_tile = lax.dynamic_slice_in_dim(gain, lax.axis_index("col") * tile, tile)
    mine_rows = tokens.shape[0]
    lanes = 128
    grid_grad = lax.all_to_all(grad_out, "col", split_axis=1, concat_axis=0, tiled=True)
    packed = jnp.concatenate(
        [
            tokens_wide.reshape(mine_rows, cols, tile),
            jnp.broadcast_to(inverse_rms[:, :, None], (mine_rows, cols, lanes)),
        ],
        axis=2,
    )
    grid = lax.all_to_all(packed, "col", split_axis=1, concat_axis=0, tiled=True)
    grid = grid.reshape(cols * mine_rows, tile + lanes)
    grid_tokens = grid[:, :tile].astype(jnp.bfloat16)
    grid_scale = grid[:, tile : tile + 1].reshape(1, cols * mine_rows)
    all_grad = row_gather(grid_grad)
    hidden_block = swiglu_grads(jnp.zeros(pre_gate.shape, jnp.float32), pre_gate, pre_up)[0]
    split = (hidden_block.shape[1] // 448) * 128
    hidden_piece = lax.all_gather(hidden_block[:, :split], "col", axis=0, tiled=True)
    partial_grad = jnp.einsum(
        "td,fd->tf", all_grad, down_weight, preferred_element_type=jnp.float32
    )
    hidden_piece, partial_grad = lax.optimization_barrier((hidden_piece, partial_grad))
    block_grad = lax.psum_scatter(partial_grad, "col", scatter_dimension=0, tiled=True)
    down_total = jnp.einsum("tf,td->fd", hidden_piece, all_grad, preferred_element_type=jnp.float32)
    down_total, block_grad = lax.optimization_barrier((down_total, block_grad))
    _, gate_block, up_block = swiglu_grads(block_grad, pre_gate, pre_up)
    all_tokens = row_gather(grid_tokens).astype(jnp.float32)
    all_scale = row_gather(grid_scale).reshape(-1, 1)
    all_normed = all_tokens * all_scale
    all_input = (all_normed * gain_tile).astype(jnp.bfloat16)
    gate_piece = lax.all_gather(gate_block, "col", axis=0, tiled=True)
    up_piece = lax.all_gather(up_block, "col", axis=0, tiled=True)
    gate_total = jnp.einsum("td,tf->df", all_input, gate_piece, preferred_element_type=jnp.float32)
    gate_total, up_piece = lax.optimization_barrier((gate_total, up_piece))
    late_block, up_piece = lax.optimization_barrier((hidden_block[:, split:], up_piece))
    late_piece = lax.all_gather(late_block, "col", axis=0, tiled=True)
    new_rows = jnp.einsum("tf,df->td", gate_piece, gate_weight, preferred_element_type=jnp.float32)
    new_rows = new_rows + jnp.einsum(
        "tf,df->td", up_piece, up_weight, preferred_element_type=jnp.float32
    )
    gain_part = jnp.sum(new_rows * all_normed, axis=0)
    tokens_all = new_rows.shape[0]
    mine = tokens_all // (rows * cols)
    blocks = new_rows.astype(jnp.bfloat16).reshape(rows * cols, mine, tile)
    gain_high = gain_part.astype(jnp.bfloat16)
    gain_low = (gain_part - gain_high.astype(jnp.float32)).astype(jnp.bfloat16)
    extra = jnp.broadcast_to(
        jnp.stack([gain_high, gain_low])[None], (rows * cols, 2, tile)
    )
    sent = jnp.concatenate([blocks, extra], axis=1)
    got = lax.all_to_all(sent, ("row", "col"), split_axis=0, concat_axis=0, tiled=True)
    got = got.reshape(rows, cols, mine + 2, tile).astype(jnp.float32)
    summed = jnp.sum(got, axis=0)
    normed_grad = summed[:, :mine, :].transpose(1, 0, 2).reshape(mine, cols * tile)
    grad_gain = (summed[:, mine, :] + summed[:, mine + 1, :]).reshape(cols * tile)
    up_total = jnp.einsum("td,tf->df", all_input, up_piece, preferred_element_type=jnp.float32)
    down_late = jnp.einsum("tf,td->fd", late_piece, all_grad, preferred_element_type=jnp.float32)
    scaled_grad = normed_grad * gain
    inner = jnp.mean(scaled_grad * normed, axis=1, keepdims=True)
    grad_tokens = (
        grad_out.astype(jnp.float32) + inverse_rms * (scaled_grad - normed * inner)
    ).astype(jnp.bfloat16)
    return (
        grad_tokens,
        grad_gain,
        gate_total.astype(jnp.bfloat16),
        up_total.astype(jnp.bfloat16),
        jnp.concatenate([down_total, down_late], axis=0).astype(jnp.bfloat16),
    )


def solution(mesh):
    in_specs = (
        P(("row", "col"), None),
        P(),
        P(("row", "col"), None),
        P("col", "row"),
        P("col", "row"),
        P("col", "row"),
        P("col", "row"),
        P("row", "col"),
    )
    out_specs = (P(("row", "col"), None), P(), P("col", "row"), P("col", "row"), P("row", "col"))
    return jax.shard_map(local, mesh=mesh, in_specs=in_specs, out_specs=out_specs, check_vma=False)
```

```python
import jax
import jax.numpy as jnp
from jax import lax
from jax.sharding import PartitionSpec as P

epsilon = 1e-05


def swiglu_grads(hidden_grad, pre_gate, pre_up):
    gate_wide = pre_gate.astype(jnp.float32)
    up_wide = pre_up.astype(jnp.float32)
    sigmoid = jax.nn.sigmoid(gate_wide)
    silu = gate_wide * sigmoid
    hidden = (silu * up_wide).astype(jnp.bfloat16)
    up_grad = (hidden_grad * silu).astype(jnp.bfloat16)
    gate_grad = (hidden_grad * up_wide * sigmoid * (1.0 + gate_wide * (1.0 - sigmoid))).astype(
        jnp.bfloat16
    )
    return (hidden, gate_grad, up_grad)


def row_gather(x):
    rows = lax.axis_size("row")
    copies = jnp.broadcast_to(x[None], (rows,) + x.shape)
    got = lax.all_to_all(copies, "row", split_axis=0, concat_axis=0, tiled=True)
    return got.reshape((rows * x.shape[0],) + x.shape[1:])


def local(tokens, gain, grad_out, pre_gate, pre_up, gate_weight, up_weight, down_weight):
    cols = lax.axis_size("col")
    rows = lax.axis_size("row")
    tokens_wide = tokens.astype(jnp.float32)
    inverse_rms = lax.rsqrt(jnp.mean(tokens_wide * tokens_wide, axis=1, keepdims=True) + epsilon)
    normed = tokens_wide * inverse_rms
    tile = gate_weight.shape[0]
    gain_tile = lax.dynamic_slice_in_dim(gain, lax.axis_index("col") * tile, tile)
    mine_rows = tokens.shape[0]
    lanes = 128
    grid_grad = lax.all_to_all(grad_out, "col", split_axis=1, concat_axis=0, tiled=True)
    packed = jnp.concatenate(
        [
            tokens_wide.reshape(mine_rows, cols, tile),
            jnp.broadcast_to(inverse_rms[:, :, None], (mine_rows, cols, lanes)),
        ],
        axis=2,
    )
    grid = lax.all_to_all(packed, "col", split_axis=1, concat_axis=0, tiled=True)
    grid = grid.reshape(cols * mine_rows, tile + lanes)
    grid_tokens = grid[:, :tile].astype(jnp.bfloat16)
    grid_scale = grid[:, tile : tile + 1].reshape(1, cols * mine_rows)
    all_grad = row_gather(grid_grad)
    hidden_block = swiglu_grads(jnp.zeros(pre_gate.shape, jnp.float32), pre_gate, pre_up)[0]
    split = (hidden_block.shape[1] // 448) * 128
    hidden_piece = lax.all_gather(hidden_block[:, :split], "col", axis=0, tiled=True)
    partial_grad = jnp.einsum(
        "td,fd->tf", all_grad, down_weight, preferred_element_type=jnp.float32
    )
    hidden_piece, partial_grad = lax.optimization_barrier((hidden_piece, partial_grad))
    block_grad = lax.psum_scatter(partial_grad, "col", scatter_dimension=0, tiled=True)
    down_total = jnp.einsum("tf,td->fd", hidden_piece, all_grad, preferred_element_type=jnp.float32)
    all_tokens = row_gather(grid_tokens).astype(jnp.float32)
    all_scale = row_gather(grid_scale).reshape(-1, 1)
    down_total, all_tokens, all_scale, block_grad = lax.optimization_barrier(
        (down_total, all_tokens, all_scale, block_grad)
    )
    _, gate_block, up_block = swiglu_grads(block_grad, pre_gate, pre_up)
    all_normed = all_tokens * all_scale
    all_input = (all_normed * gain_tile).astype(jnp.bfloat16)
    gate_piece = lax.all_gather(gate_block, "col", axis=0, tiled=True)
    up_piece = lax.all_gather(up_block, "col", axis=0, tiled=True)
    gate_total = jnp.einsum("td,tf->df", all_input, gate_piece, preferred_element_type=jnp.float32)
    gate_total, up_piece = lax.optimization_barrier((gate_total, up_piece))
    late_block, up_piece = lax.optimization_barrier((hidden_block[:, split:], up_piece))
    late_piece = lax.all_gather(late_block, "col", axis=0, tiled=True)
    new_rows = jnp.einsum("tf,df->td", gate_piece, gate_weight, preferred_element_type=jnp.float32)
    new_rows = new_rows + jnp.einsum(
        "tf,df->td", up_piece, up_weight, preferred_element_type=jnp.float32
    )
    gain_part = jnp.sum(new_rows * all_normed, axis=0)
    tokens_all = new_rows.shape[0]
    blocks = new_rows.astype(jnp.bfloat16).reshape(rows, tokens_all // rows, tile)
    gain_high = gain_part.astype(jnp.bfloat16)
    gain_low = (gain_part - gain_high.astype(jnp.float32)).astype(jnp.bfloat16)
    extra = jnp.zeros((rows, 8, tile), jnp.bfloat16)
    extra = extra.at[:, 0, :].set(gain_high).at[:, 1, :].set(gain_low)
    sent = jnp.concatenate([blocks, extra], axis=1)
    got = lax.all_to_all(sent, "row", split_axis=0, concat_axis=0, tiled=True)
    summed = jnp.sum(got.astype(jnp.float32), axis=0)
    grid_back = summed[: tokens_all // rows]
    gain_tile_grad = summed[tokens_all // rows] + summed[tokens_all // rows + 1]
    per_col = grid_back.reshape(cols, -1, tile)
    mine = per_col.shape[1]
    sent2 = jnp.concatenate(
        [per_col, jnp.broadcast_to(gain_tile_grad[None, None, :], (cols, 1, tile))], axis=1
    )
    got2 = lax.all_to_all(sent2, "col", split_axis=0, concat_axis=0, tiled=True)
    normed_grad = got2[:, :mine, :].transpose(1, 0, 2).reshape(mine, cols * tile)
    grad_gain = got2[:, mine, :].reshape(cols * tile)
    up_total = jnp.einsum("td,tf->df", all_input, up_piece, preferred_element_type=jnp.float32)
    down_late = jnp.einsum("tf,td->fd", late_piece, all_grad, preferred_element_type=jnp.float32)
    scaled_grad = normed_grad * gain
    inner = jnp.mean(scaled_grad * normed, axis=1, keepdims=True)
    grad_tokens = (
        grad_out.astype(jnp.float32) + inverse_rms * (scaled_grad - normed * inner)
    ).astype(jnp.bfloat16)
    return (
        grad_tokens,
        grad_gain,
        gate_total.astype(jnp.bfloat16),
        up_total.astype(jnp.bfloat16),
        jnp.concatenate([down_total, down_late], axis=0).astype(jnp.bfloat16),
    )


def solution(mesh):
    in_specs = (
        P(("row", "col"), None),
        P(),
        P(("row", "col"), None),
        P("col", "row"),
        P("col", "row"),
        P("col", "row"),
        P("col", "row"),
        P("row", "col"),
    )
    out_specs = (P(("row", "col"), None), P(), P("col", "row"), P("col", "row"), P("row", "col"))
    return jax.shard_map(local, mesh=mesh, in_specs=in_specs, out_specs=out_specs, check_vma=False)
```

```python
import jax
import jax.numpy as jnp
from jax import lax
from jax.sharding import PartitionSpec as P

epsilon = 1e-05


def swiglu_grads(hidden_grad, pre_gate, pre_up):
    gate_wide = pre_gate.astype(jnp.float32)
    up_wide = pre_up.astype(jnp.float32)
    sigmoid = jax.nn.sigmoid(gate_wide)
    silu = gate_wide * sigmoid
    hidden = (silu * up_wide).astype(jnp.bfloat16)
    up_grad = (hidden_grad * silu).astype(jnp.bfloat16)
    gate_grad = (hidden_grad * up_wide * sigmoid * (1.0 + gate_wide * (1.0 - sigmoid))).astype(
        jnp.bfloat16
    )
    return (hidden, gate_grad, up_grad)


def row_gather(x):
    rows = lax.axis_size("row")
    copies = jnp.broadcast_to(x[None], (rows,) + x.shape)
    got = lax.all_to_all(copies, "row", split_axis=0, concat_axis=0, tiled=True)
    return got.reshape((rows * x.shape[0],) + x.shape[1:])


def local(tokens, gain, grad_out, pre_gate, pre_up, gate_weight, up_weight, down_weight):
    cols = lax.axis_size("col")
    rows = lax.axis_size("row")
    tokens_wide = tokens.astype(jnp.float32)
    inverse_rms = lax.rsqrt(jnp.mean(tokens_wide * tokens_wide, axis=1, keepdims=True) + epsilon)
    normed = tokens_wide * inverse_rms
    tile = gate_weight.shape[0]
    gain_tile = lax.dynamic_slice_in_dim(gain, lax.axis_index("col") * tile, tile)
    mine_rows = tokens.shape[0]
    lanes = 128
    grid_grad = lax.all_to_all(grad_out, "col", split_axis=1, concat_axis=0, tiled=True)
    packed = jnp.concatenate(
        [
            tokens_wide.reshape(mine_rows, cols, tile),
            jnp.broadcast_to(inverse_rms[:, :, None], (mine_rows, cols, lanes)),
        ],
        axis=2,
    )
    grid = lax.all_to_all(packed, "col", split_axis=1, concat_axis=0, tiled=True)
    grid = grid.reshape(cols * mine_rows, tile + lanes)
    grid_tokens = grid[:, :tile].astype(jnp.bfloat16)
    grid_scale = grid[:, tile : tile + 1].reshape(1, cols * mine_rows)
    all_grad = row_gather(grid_grad)
    hidden_block = swiglu_grads(jnp.zeros(pre_gate.shape, jnp.float32), pre_gate, pre_up)[0]
    split = (hidden_block.shape[1] // 512) * 128
    hidden_piece = lax.all_gather(hidden_block[:, :split], "col", axis=0, tiled=True)
    partial_grad = jnp.einsum(
        "td,fd->tf", all_grad, down_weight, preferred_element_type=jnp.float32
    )
    hidden_piece, partial_grad = lax.optimization_barrier((hidden_piece, partial_grad))
    block_grad = lax.psum_scatter(partial_grad, "col", scatter_dimension=0, tiled=True)
    down_total = jnp.einsum("tf,td->fd", hidden_piece, all_grad, preferred_element_type=jnp.float32)
    down_total, block_grad = lax.optimization_barrier((down_total, block_grad))
    _, gate_block, up_block = swiglu_grads(block_grad, pre_gate, pre_up)
    all_tokens = row_gather(grid_tokens).astype(jnp.float32)
    all_scale = row_gather(grid_scale).reshape(-1, 1)
    all_normed = all_tokens * all_scale
    all_input = (all_normed * gain_tile).astype(jnp.bfloat16)
    gate_piece = lax.all_gather(gate_block, "col", axis=0, tiled=True)
    up_piece = lax.all_gather(up_block, "col", axis=0, tiled=True)
    gate_total = jnp.einsum("td,tf->df", all_input, gate_piece, preferred_element_type=jnp.float32)
    gate_total, up_piece = lax.optimization_barrier((gate_total, up_piece))
    late_block, up_piece = lax.optimization_barrier((hidden_block[:, split:], up_piece))
    late_piece = lax.all_gather(late_block, "col", axis=0, tiled=True)
    new_rows = jnp.einsum("tf,df->td", gate_piece, gate_weight, preferred_element_type=jnp.float32)
    new_rows = new_rows + jnp.einsum(
        "tf,df->td", up_piece, up_weight, preferred_element_type=jnp.float32
    )
    gain_part = jnp.sum(new_rows * all_normed, axis=0)
    tokens_all = new_rows.shape[0]
    blocks = new_rows.astype(jnp.bfloat16).reshape(rows, tokens_all // rows, tile)
    gain_high = gain_part.astype(jnp.bfloat16)
    gain_low = (gain_part - gain_high.astype(jnp.float32)).astype(jnp.bfloat16)
    extra = jnp.zeros((rows, 8, tile), jnp.bfloat16)
    extra = extra.at[:, 0, :].set(gain_high).at[:, 1, :].set(gain_low)
    sent = jnp.concatenate([blocks, extra], axis=1)
    got = lax.all_to_all(sent, "row", split_axis=0, concat_axis=0, tiled=True)
    summed = jnp.sum(got.astype(jnp.float32), axis=0)
    grid_back = summed[: tokens_all // rows]
    gain_tile_grad = summed[tokens_all // rows] + summed[tokens_all // rows + 1]
    per_col = grid_back.reshape(cols, -1, tile)
    mine = per_col.shape[1]
    sent2 = jnp.concatenate(
        [per_col, jnp.broadcast_to(gain_tile_grad[None, None, :], (cols, 1, tile))], axis=1
    )
    got2 = lax.all_to_all(sent2, "col", split_axis=0, concat_axis=0, tiled=True)
    normed_grad = got2[:, :mine, :].transpose(1, 0, 2).reshape(mine, cols * tile)
    grad_gain = got2[:, mine, :].reshape(cols * tile)
    up_total = jnp.einsum("td,tf->df", all_input, up_piece, preferred_element_type=jnp.float32)
    down_late = jnp.einsum("tf,td->fd", late_piece, all_grad, preferred_element_type=jnp.float32)
    scaled_grad = normed_grad * gain
    inner = jnp.mean(scaled_grad * normed, axis=1, keepdims=True)
    grad_tokens = (
        grad_out.astype(jnp.float32) + inverse_rms * (scaled_grad - normed * inner)
    ).astype(jnp.bfloat16)
    return (
        grad_tokens,
        grad_gain,
        gate_total.astype(jnp.bfloat16),
        up_total.astype(jnp.bfloat16),
        jnp.concatenate([down_total, down_late], axis=0).astype(jnp.bfloat16),
    )


def solution(mesh):
    in_specs = (
        P(("row", "col"), None),
        P(),
        P(("row", "col"), None),
        P("col", "row"),
        P("col", "row"),
        P("col", "row"),
        P("col", "row"),
        P("row", "col"),
    )
    out_specs = (P(("row", "col"), None), P(), P("col", "row"), P("col", "row"), P("row", "col"))
    return jax.shard_map(local, mesh=mesh, in_specs=in_specs, out_specs=out_specs, check_vma=False)
```
